128 devices in a mesh: head: 8 (over x, core), tail: 16 (over y, z).
Axes of the slice: x: 4, y: 4, z: 4, core: 2. Of those that a mesh axis runs over, the one named last changes fastest.
Arguments:
- head_table: float32 [8, 4096, 400], P('head', 'tail'), may hold values from -4 to 4
- tail_table: float32 [16, 4096, 400], P('tail', 'head'), may hold values from -4 to 4
- relations: float32 [7424, 400], replicated, may hold values from -4 to 4
- edges: int32 [8, 16, 3, 640], P('head', 'tail'), may hold values from 0 to 7423, as said below
- bucket_size: int32 [8, 16], P('head', 'tail'), may hold values from 160 to 640, as said below
- head_touched: int32 [8, 16, 16], P('head', 'tail'), may hold values from -1 to 31, as said below
- tail_touched: int32 [8, 16, 16], P('head', 'tail'), may hold values from -1 to 31, as said below
- negatives: int32 [8, 16, 1, 2, 1000], P('head', 'tail'), may hold values from 0 to 2047, as said below
Outputs:
- head_grad: float32 [8, 4096, 400], P('head', 'tail')
- tail_grad: float32 [16, 4096, 400], P('tail', 'head')
- relation_grad: float32 [7424, 400], P(('head', 'tail'))
The draws below stay inside these ranges and needn't reach their ends.
Inputs may be any that keep to these rules, and one draw needn't show every extreme that they name: `head_touched`: slot s of a bucket names a block of the head partition that is stored at index s // 1 of tail (block k covers partition rows 128 k to 128 k + 127, stored at index k // 2), or is -1; the slots of one storing device differ. In each row of the grid one bucket uses every slot, and one storing index is asked by every bucket of that row for as many blocks as it has slots there, 1. `tail_touched`: slot s names a block of the tail partition stored at index s // 2 of head (block k at index k // 4 with 4 = 4), or is -1; the slots of one storing device differ. In each column of the grid one bucket uses every slot, and one storing index is asked by every bucket of that column for as many blocks as it has slots there, 2. edges[a, b, 0, e] = 128 s + i names row i of head slot s of the bucket, a slot that is not -1; edges[a, b, 2, e] names a tail slot row the same way; edges[a, b, 1, e] is a relation below 7424. negatives[a, b, c, 0, j] are head ids and negatives[a, b, c, 1, j] tail ids, read as in edges. `bucket_size`: edges at positions at or beyond it are ignored; some bucket holds 640.
All inputs are finite; a program needn't handle non-finite values.
Results may differ from the reference program's by a relative error of at most 0.0003.
Values sent between devices are 32-bit elements; how exact they have to be, the bound alone decides.
No kernel may reach another device: no remote copies, remote signals or barrier semaphores. Data moves between devices by JAX's collectives and lax.ppermute only.
A program may use at most 192 MiB of HBM per device.

```python
import jax
import jax.numpy as jnp
from jax import lax

D = 400
NREL = 7424
HBLK = 2
HCAP = 1
TCAP = 2
SPAN = 640
NEG = 1000
SPANS = 1
HPARTS = 8
TPARTS = 16
PART = 4096
EDGES = 640


def entity_rows(key, salt_value, array_shape):
    k_scale, k_noise = jax.random.split(jax.random.fold_in(key, salt_value), 2)
    row_shape = array_shape[:-1] + (1,)
    row_scale = jnp.exp(jax.random.uniform(k_scale, row_shape, jnp.float32, jnp.log(0.3), jnp.log(3.0)))
    return jnp.clip(jax.random.normal(k_noise, array_shape, jnp.float32) * row_scale * 0.15, -4.0, 4.0)


def draw_head_table(key, part):
    return entity_rows(key, 41, (HPARTS, PART, D))


def draw_tail_table(key, part):
    return entity_rows(key, 42, (TPARTS, PART, D))


def draw_relations(key, part):
    k_scale, k_real = jax.random.split(jax.random.fold_in(key, 43), 2)
    row_scale = jnp.exp(jax.random.uniform(k_scale, (NREL, 1), jnp.float32, jnp.log(0.5), jnp.log(2.0)))
    return jnp.clip(jax.random.normal(k_real, (NREL, D), jnp.float32) * 0.6 * row_scale, -4.0, 4.0)


def owner_slots(key, groups, members, owners, per_owner, block_list):
    k_order, k_rate, k_live, k_owner, k_member = jax.random.split(key, 5)
    ranking = jax.random.randint(k_order, (groups, members, owners, block_list), 0, 1 << 20) * block_list
    ranking = ranking + jnp.arange(block_list, dtype=jnp.int32)
    chosen = jnp.argsort(ranking, axis=-1)[..., :per_owner].astype(jnp.int32)
    rate_level = jax.random.randint(k_rate, (groups, members, 1, 1), 3, 8)
    live_slot = jax.random.randint(k_live, (groups, members, owners, per_owner), 0, 8) < rate_level
    busy_owner = jax.random.randint(k_owner, (groups, 1, 1, 1), 0, owners)
    busy_member = jax.random.randint(k_member, (groups, 1, 1, 1), 0, members)
    owner_index = jnp.arange(owners, dtype=jnp.int32)[None, None, :, None]
    member_index = jnp.arange(members, dtype=jnp.int32)[None, :, None, None]
    live_slot = live_slot | (owner_index == busy_owner) | (member_index == busy_member)
    named = jnp.where(live_slot, owner_index * block_list + chosen, -1)
    return named.reshape(groups, members, owners * per_owner).astype(jnp.int32)


def grid_layout(key):
    head_slots = owner_slots(jax.random.fold_in(key, 11), HPARTS, TPARTS, TPARTS, HCAP, HBLK)
    tail_blocks = HBLK * TPARTS // HPARTS
    tail_slots = owner_slots(jax.random.fold_in(key, 12), TPARTS, HPARTS, HPARTS, TCAP, tail_blocks)
    return (head_slots, jnp.transpose(tail_slots, (1, 0, 2)))


def pick_rows(key, touched, extra_shape):
    live_slot = (touched >= 0).astype(jnp.int32)
    live_total = jnp.sum(live_slot, axis=-1)
    running = jnp.cumsum(live_slot, axis=-1)
    k_rank, k_row = jax.random.split(key)
    full_shape = touched.shape[:2] + extra_shape
    padding = (1,) * len(extra_shape)
    ranks = jax.random.randint(k_rank, full_shape, 0, 1 << 20) % live_total.reshape(touched.shape[:2] + padding)
    running = running.reshape(touched.shape[:2] + padding + (touched.shape[2],))
    slot_index = jnp.sum((running <= ranks[..., None]).astype(jnp.int32), axis=-1)
    return (slot_index * 128 + jax.random.randint(k_row, full_shape, 0, 128)).astype(jnp.int32)


def draw_head_touched(key, part):
    return grid_layout(key)[0]


def draw_tail_touched(key, part):
    return grid_layout(key)[1]


def draw_edges(key, part):
    head_slots, tail_slots = grid_layout(key)
    head_ids = pick_rows(jax.random.fold_in(key, 21), head_slots, (EDGES,))
    tail_ids = pick_rows(jax.random.fold_in(key, 22), tail_slots, (EDGES,))
    k_first, k_second, k_order = jax.random.split(jax.random.fold_in(key, 23), 3)
    first_pick = jax.random.randint(k_first, (HPARTS, TPARTS, EDGES), 0, NREL)
    second_pick = jax.random.randint(k_second, (HPARTS, TPARTS, EDGES), 0, NREL)
    relation_order = jax.random.permutation(k_order, NREL).astype(jnp.int32)
    relation_ids = relation_order[first_pick * second_pick // NREL]
    relation_ids = relation_ids.at[0, 0, 0].set(NREL - 1)
    return jnp.stack([head_ids, relation_ids, tail_ids], axis=2).astype(jnp.int32)


def draw_negatives(key, part):
    head_slots, tail_slots = grid_layout(key)
    head_ids = pick_rows(jax.random.fold_in(key, 24), head_slots, (SPANS, NEG))
    tail_ids = pick_rows(jax.random.fold_in(key, 25), tail_slots, (SPANS, NEG))
    return jnp.stack([head_ids, tail_ids], axis=3).astype(jnp.int32)


def draw_bucket_size(key, part):
    k_size, k_full = jax.random.split(jax.random.fold_in(key, 31))
    drawn_sizes = jax.random.randint(k_size, (HPARTS, TPARTS), EDGES // 4, EDGES + 1)
    full_device = jax.random.randint(k_full, (), 0, HPARTS * TPARTS)
    flat_index = jnp.arange(HPARTS * TPARTS, dtype=jnp.int32).reshape(HPARTS, TPARTS)
    return jnp.where(flat_index == full_device, EDGES, drawn_sizes).astype(jnp.int32)


def setup_inputs(seed: int = 0) -> dict:
    key_list = jax.random.split(jax.random.key(seed), 9)
    head_table = draw_head_table(jax.random.fold_in(key_list[8], 71), 0)
    tail_table = draw_tail_table(jax.random.fold_in(key_list[8], 71), 0)
    relations = draw_relations(jax.random.fold_in(key_list[8], 71), 0)
    edges = draw_edges(jax.random.fold_in(key_list[8], 71), 0)
    bucket_size = draw_bucket_size(jax.random.fold_in(key_list[8], 71), 0)
    head_touched = draw_head_touched(jax.random.fold_in(key_list[8], 71), 0)
    tail_touched = draw_tail_touched(jax.random.fold_in(key_list[8], 71), 0)
    negatives = draw_negatives(jax.random.fold_in(key_list[8], 71), 0)
    return {"head_table": head_table, "tail_table": tail_table, "relations": relations, "edges": edges, "bucket_size": bucket_size, "head_touched": head_touched, "tail_touched": tail_touched, "negatives": negatives}


TOP_PRECISION = lax.Precision.HIGHEST

def rotate_query(head_vec, rel_vec):
    middle = head_vec.shape[1] // 2
    head_re, head_im = (head_vec[:, :middle], head_vec[:, middle:])
    rel_re, rel_im = (rel_vec[:, :middle], rel_vec[:, middle:])
    return jnp.concatenate([head_re * rel_re + head_im * rel_im, head_im * rel_re - head_re * rel_im], axis=1)

def rotate_tail(rel_vec, tail_vec):
    middle = tail_vec.shape[1] // 2
    tail_re, tail_im = (tail_vec[:, :middle], tail_vec[:, middle:])
    rel_re, rel_im = (rel_vec[:, :middle], rel_vec[:, middle:])
    return jnp.concatenate([rel_re * tail_re - rel_im * tail_im, rel_re * tail_im + rel_im * tail_re], axis=1)

def side_terms(query_vec, positive, candidates):
    scores = jnp.dot(query_vec, candidates.T, precision=TOP_PRECISION)
    weights = lax.stop_gradient(jax.nn.softmax(scores, axis=1))
    return jax.nn.softplus(-positive) + lax.optimization_barrier(jnp.sum(weights * jax.nn.softplus(scores), axis=1))

def edge_loss(head_rows, tail_rows, rel_rows, edge_ids, live_count, negative_ids):
    summed = jnp.zeros((), jnp.float32)
    for span_no in range(SPANS):
        offset = span_no * SPAN
        head_vec = head_rows[edge_ids[0, offset:offset + SPAN]]
        tail_vec = tail_rows[edge_ids[2, offset:offset + SPAN]]
        rel_vec = rel_rows[offset:offset + SPAN]
        query_vec = rotate_query(head_vec, rel_vec)
        tail_image = rotate_tail(rel_vec, tail_vec)
        positive = lax.optimization_barrier(jnp.sum(query_vec * tail_vec, axis=1))
        tail_side = side_terms(query_vec, positive, tail_rows[negative_ids[span_no, 1]])
        head_side = side_terms(tail_image, positive, head_rows[negative_ids[span_no, 0]])
        live_mask = (jnp.arange(SPAN, dtype=jnp.int32) + offset < live_count).astype(jnp.float32)
        summed = summed + jnp.sum(live_mask * (tail_side + head_side))
    return summed

def gather_slots(partition_rows, slot_blocks):
    block_list = partition_rows.reshape(-1, 128, partition_rows.shape[1])
    row_selector = (slot_blocks[:, None] == jnp.arange(block_list.shape[0], dtype=jnp.int32)[None, :]).astype(jnp.float32)
    return jnp.einsum('il,lov->iov', row_selector, block_list, precision=TOP_PRECISION).reshape(-1, partition_rows.shape[1])

def reference(head_table, tail_table, relations, edges, bucket_size, head_touched, tail_touched, negatives):

    def device_step(carry, device):
        head_acc, tail_acc, rel_acc = carry
        head_part = device // TPARTS
        tail_part = device % TPARTS
        edge_ids = edges[head_part, tail_part]

        def local_loss(head_source, tail_source, rel_table):
            head_rows = gather_slots(head_source, head_touched[head_part, tail_part])
            tail_rows = gather_slots(tail_source, tail_touched[head_part, tail_part])
            return edge_loss(head_rows, tail_rows, rel_table[edge_ids[1]], edge_ids, bucket_size[head_part, tail_part], negatives[head_part, tail_part])
        loss_value, pullback = jax.vjp(local_loss, head_table[head_part], tail_table[tail_part], relations)
        head_piece, tail_piece, rel_piece = pullback(jnp.ones_like(loss_value))
        return ((head_acc.at[head_part].add(head_piece), tail_acc.at[tail_part].add(tail_piece), rel_acc + rel_piece), None)
    start_state = (jnp.zeros_like(head_table), jnp.zeros_like(tail_table), jnp.zeros_like(relations))
    final_state, unused = lax.scan(device_step, start_state, jnp.arange(HPARTS * TPARTS, dtype=jnp.int32))
    return (final_state[0], final_state[1], final_state[2])
```

```python
import jax
import jax.numpy as jnp
from jax import lax
from jax.sharding import PartitionSpec as P

SPAN = 640


TOP_PRECISION = lax.Precision.HIGHEST


def rotate_query(head_vec, rel_vec):
    middle = head_vec.shape[1] // 2
    head_re, head_im = (head_vec[:, :middle], head_vec[:, middle:])
    rel_re, rel_im = (rel_vec[:, :middle], rel_vec[:, middle:])
    return jnp.concatenate(
        [head_re * rel_re + head_im * rel_im, head_im * rel_re - head_re * rel_im], axis=1
    )


def rotate_tail(rel_vec, tail_vec):
    middle = tail_vec.shape[1] // 2
    tail_re, tail_im = (tail_vec[:, :middle], tail_vec[:, middle:])
    rel_re, rel_im = (rel_vec[:, :middle], rel_vec[:, middle:])
    return jnp.concatenate(
        [rel_re * tail_re - rel_im * tail_im, rel_re * tail_im + rel_im * tail_re], axis=1
    )


def side_terms(query_vec, positive, candidates):
    scores = jnp.dot(query_vec, candidates.T, precision=TOP_PRECISION)
    weights = lax.stop_gradient(jax.nn.softmax(scores, axis=1))
    return jax.nn.softplus(-positive) + jnp.sum(weights * jax.nn.softplus(scores), axis=1)


def edge_loss(head_rows, tail_rows, rel_rows, edge_ids, live_count, negative_ids):
    head_vec = head_rows[edge_ids[0, 0:SPAN]]
    tail_vec = tail_rows[edge_ids[2, 0:SPAN]]
    query_vec = rotate_query(head_vec, rel_rows)
    tail_image = rotate_tail(rel_rows, tail_vec)
    positive = jnp.sum(query_vec * tail_vec, axis=1)
    tail_side = side_terms(query_vec, positive, tail_rows[negative_ids[0, 1]])
    head_side = side_terms(tail_image, positive, head_rows[negative_ids[0, 0]])
    live_mask = (jnp.arange(SPAN, dtype=jnp.int32) + 0 < live_count).astype(jnp.float32)
    summed = jnp.sum(live_mask * (tail_side + head_side))
    return summed


def one_hot_rows(block_ids, choices_count):
    return (block_ids[..., None] == jnp.arange(choices_count, dtype=jnp.int32)).astype(jnp.float32)


def shards(
    head_table, tail_table, relations, edges, bucket_size, head_touched, tail_touched, negatives
):
    feature_columns = head_table.shape[2]
    head_count = lax.axis_size("head")
    tail_count = lax.axis_size("tail")
    head_slots = head_touched[0, 0]
    tail_slots = tail_touched[0, 0]
    head_complete = lax.all_gather(head_table[0], "tail", axis=0, tiled=True)
    head_selector = one_hot_rows(head_slots, head_complete.shape[0] // 128)
    head_rows = jnp.einsum(
        "il,lov->iov",
        head_selector,
        head_complete.reshape(-1, 128, feature_columns),
        precision=TOP_PRECISION,
    )
    tail_complete = lax.all_gather(tail_table[0], "head", axis=0, tiled=True)
    tail_selector = one_hot_rows(tail_slots, tail_complete.shape[0] // 128)
    tail_rows = jnp.einsum(
        "il,lov->iov",
        tail_selector,
        tail_complete.reshape(-1, 128, feature_columns),
        precision=TOP_PRECISION,
    )
    edge_ids = edges[0, 0]
    relation_ids = edge_ids[1]
    rel_rows = relations[relation_ids]

    def local_loss(head_flat, tail_flat, rel_flat):
        return edge_loss(
            head_flat, tail_flat, rel_flat, edge_ids, bucket_size[0, 0], negatives[0, 0]
        )

    loss_value, pullback = jax.vjp(
        local_loss,
        head_rows.reshape(-1, feature_columns),
        tail_rows.reshape(-1, feature_columns),
        rel_rows,
    )
    head_slot_gradient, tail_slot_gradient, rel_edge_grad = pullback(jnp.ones_like(loss_value))
    head_slot_gradient = head_slot_gradient.reshape(-1, 128, feature_columns)
    tail_slot_gradient = tail_slot_gradient.reshape(-1, 128, feature_columns)
    head_full_rows = jnp.einsum(
        "ip,iey->pey", head_selector, head_slot_gradient, precision=TOP_PRECISION
    ).reshape(-1, feature_columns)
    head_result = lax.psum_scatter(head_full_rows, "tail", scatter_dimension=0, tiled=True)
    tail_full_rows = jnp.einsum(
        "ip,iey->pey", tail_selector, tail_slot_gradient, precision=TOP_PRECISION
    ).reshape(-1, feature_columns)
    tail_result = lax.psum_scatter(tail_full_rows, "head", scatter_dimension=0, tiled=True)
    row_count = relations.shape[0]
    per = row_count // (head_count * tail_count)
    dense = jnp.zeros((head_count, tail_count * per, feature_columns), jnp.float32).at[relation_ids // (tail_count * per), relation_ids % (tail_count * per)].add(rel_edge_grad)
    stage = lax.psum_scatter(dense, "head", scatter_dimension=0, tiled=True).reshape(tail_count, per, feature_columns)
    relation_result = lax.psum_scatter(stage, "tail", scatter_dimension=0, tiled=True).reshape(-1, feature_columns)
    return (
        head_result.reshape(1, -1, feature_columns),
        tail_result.reshape(1, -1, feature_columns),
        relation_result,
    )


def solution(mesh):
    in_specs = (
        P("head", "tail", None),
        P("tail", "head", None),
        P(),
        P("head", "tail", None, None),
        P("head", "tail"),
        P("head", "tail", None),
        P("head", "tail", None),
        P("head", "tail", None, None, None),
    )
    out_specs = (P("head", "tail", None), P("tail", "head", None), P(("head", "tail"), None))
    return jax.shard_map(shards, mesh=mesh, in_specs=in_specs, out_specs=out_specs, check_vma=False)
```

```python
import jax
import jax.numpy as jnp
from jax import lax
from jax.sharding import PartitionSpec as P

SPAN = 640


TOP_PRECISION = lax.Precision.HIGHEST


def rotate_query(head_vec, rel_vec):
    middle = head_vec.shape[1] // 2
    head_re, head_im = (head_vec[:, :middle], head_vec[:, middle:])
    rel_re, rel_im = (rel_vec[:, :middle], rel_vec[:, middle:])
    return jnp.concatenate(
        [head_re * rel_re + head_im * rel_im, head_im * rel_re - head_re * rel_im], axis=1
    )


def rotate_tail(rel_vec, tail_vec):
    middle = tail_vec.shape[1] // 2
    tail_re, tail_im = (tail_vec[:, :middle], tail_vec[:, middle:])
    rel_re, rel_im = (rel_vec[:, :middle], rel_vec[:, middle:])
    return jnp.concatenate(
        [rel_re * tail_re - rel_im * tail_im, rel_re * tail_im + rel_im * tail_re], axis=1
    )


def side_terms(query_vec, positive, candidates):
    scores = jnp.dot(query_vec, candidates.T, precision=TOP_PRECISION)
    weights = lax.stop_gradient(jax.nn.softmax(scores, axis=1))
    return jax.nn.softplus(-positive) + jnp.sum(weights * jax.nn.softplus(scores), axis=1)


def edge_loss(head_rows, tail_rows, rel_rows, edge_ids, live_count, negative_ids):
    head_vec = head_rows[edge_ids[0, 0:SPAN]]
    tail_vec = tail_rows[edge_ids[2, 0:SPAN]]
    query_vec = rotate_query(head_vec, rel_rows)
    tail_image = rotate_tail(rel_rows, tail_vec)
    positive = jnp.sum(query_vec * tail_vec, axis=1)
    tail_side = side_terms(query_vec, positive, tail_rows[negative_ids[0, 1]])
    head_side = side_terms(tail_image, positive, head_rows[negative_ids[0, 0]])
    live_mask = (jnp.arange(SPAN, dtype=jnp.int32) + 0 < live_count).astype(jnp.float32)
    summed = jnp.sum(live_mask * (tail_side + head_side))
    return summed


def one_hot_rows(block_ids, choices_count):
    return (block_ids[..., None] == jnp.arange(choices_count, dtype=jnp.int32)).astype(jnp.float32)


def shards(
    head_table, tail_table, relations, edges, bucket_size, head_touched, tail_touched, negatives
):
    feature_columns = head_table.shape[2]
    head_count = lax.axis_size("head")
    tail_count = lax.axis_size("tail")
    tail_index = lax.axis_index("tail")
    head_slots = head_touched[0, 0]
    tail_slots = tail_touched[0, 0]

    local_blocks = head_table[0].reshape(-1, 128, feature_columns)
    blocks_here = local_blocks.shape[0]
    asked = lax.all_gather(head_slots, "tail", axis=0)[:, tail_index]
    shifts = jnp.arange(tail_count, dtype=jnp.int32)
    asker = (tail_index + shifts) % tail_count
    giver = (tail_index - shifts) % tail_count
    sent_block = jnp.clip(asked - tail_index * blocks_here, 0, blocks_here - 1)
    pieces = [local_blocks[sent_block[tail_index]]]
    for shift in range(1, tail_count):
        pairs = [(i, (i + shift) % tail_count) for i in range(tail_count)]
        pieces.append(lax.ppermute(local_blocks[sent_block[asker[shift]]], "tail", pairs))
    by_shift = jnp.stack(pieces)
    head_rows = jnp.take(by_shift, giver, axis=0)
    head_rows = jnp.where((head_slots >= 0)[:, None, None], head_rows, 0.0)

    tail_complete = lax.all_gather(tail_table[0], "head", axis=0, tiled=True)
    tail_selector = one_hot_rows(tail_slots, tail_complete.shape[0] // 128)
    tail_rows = jnp.einsum(
        "il,lov->iov",
        tail_selector,
        tail_complete.reshape(-1, 128, feature_columns),
        precision=TOP_PRECISION,
    )
    edge_ids = edges[0, 0]
    relation_ids = edge_ids[1]
    rel_rows = relations[relation_ids]

    def local_loss(head_flat, tail_flat, rel_flat):
        return edge_loss(
            head_flat, tail_flat, rel_flat, edge_ids, bucket_size[0, 0], negatives[0, 0]
        )

    loss_value, pullback = jax.vjp(
        local_loss,
        head_rows.reshape(-1, feature_columns),
        tail_rows.reshape(-1, feature_columns),
        rel_rows,
    )
    head_slot_gradient, tail_slot_gradient, rel_edge_grad = pullback(jnp.ones_like(loss_value))

    row_count = relations.shape[0]
    per_device = row_count // (head_count * tail_count)
    dense = jax.ops.segment_sum(rel_edge_grad, relation_ids, num_segments=row_count)
    stage = lax.psum_scatter(
        dense.reshape(head_count, tail_count * per_device, feature_columns),
        "head",
        scatter_dimension=0,
        tiled=True,
    ).reshape(tail_count, per_device, feature_columns)

    head_slot_gradient = jnp.where(
        (head_slots >= 0)[:, None, None],
        head_slot_gradient.reshape(-1, 128, feature_columns),
        0.0,
    )
    returned = [head_slot_gradient[tail_index]]
    for shift in range(1, tail_count):
        pairs = [(i, (i + shift) % tail_count) for i in range(tail_count)]
        returned.append(lax.ppermute(head_slot_gradient[asker[shift]], "tail", pairs))
    returned = jnp.stack(returned)
    returned_block = asked[giver] - tail_index * blocks_here
    head_result = jnp.stack(
        [
            jnp.sum(jnp.where((returned_block == j)[:, None, None], returned, 0.0), axis=0)
            for j in range(blocks_here)
        ]
    ).reshape(-1, feature_columns)

    tail_slot_gradient = tail_slot_gradient.reshape(-1, 128, feature_columns)
    tail_full_rows = jnp.einsum(
        "ip,iey->pey", tail_selector, tail_slot_gradient, precision=TOP_PRECISION
    ).reshape(-1, feature_columns)
    tail_result = lax.psum_scatter(tail_full_rows, "head", scatter_dimension=0, tiled=True)

    relation_result = stage[tail_index]
    for shift in range(1, tail_count):
        pairs = [(i, (i + shift) % tail_count) for i in range(tail_count)]
        relation_result = relation_result + lax.ppermute(stage[asker[shift]], "tail", pairs)
    return (
        head_result.reshape(1, -1, feature_columns),
        tail_result.reshape(1, -1, feature_columns),
        relation_result,
    )


def solution(mesh):
    in_specs = (
        P("head", "tail", None),
        P("tail", "head", None),
        P(),
        P("head", "tail", None, None),
        P("head", "tail"),
        P("head", "tail", None),
        P("head", "tail", None),
        P("head", "tail", None, None, None),
    )
    out_specs = (P("head", "tail", None), P("tail", "head", None), P(("head", "tail"), None))
    return jax.shard_map(shards, mesh=mesh, in_specs=in_specs, out_specs=out_specs, check_vma=False)
```

```python
import jax
import jax.numpy as jnp
from jax import lax
from jax.sharding import PartitionSpec as P

SPAN = 640


TOP_PRECISION = lax.Precision.HIGHEST


def rotate_query(head_vec, rel_vec):
    middle = head_vec.shape[1] // 2
    head_re, head_im = (head_vec[:, :middle], head_vec[:, middle:])
    rel_re, rel_im = (rel_vec[:, :middle], rel_vec[:, middle:])
    return jnp.concatenate(
        [head_re * rel_re + head_im * rel_im, head_im * rel_re - head_re * rel_im], axis=1
    )


def rotate_tail(rel_vec, tail_vec):
    middle = tail_vec.shape[1] // 2
    tail_re, tail_im = (tail_vec[:, :middle], tail_vec[:, middle:])
    rel_re, rel_im = (rel_vec[:, :middle], rel_vec[:, middle:])
    return jnp.concatenate(
        [rel_re * tail_re - rel_im * tail_im, rel_re * tail_im + rel_im * tail_re], axis=1
    )


def side_terms(query_vec, positive, candidates):
    scores = jnp.dot(query_vec, candidates.T, precision=TOP_PRECISION)
    weights = lax.stop_gradient(jax.nn.softmax(scores, axis=1))
    return jax.nn.softplus(-positive) + jnp.sum(weights * jax.nn.softplus(scores), axis=1)


def edge_loss(head_rows, tail_rows, rel_rows, edge_ids, live_count, negative_ids):
    head_vec = head_rows[edge_ids[0, 0:SPAN]]
    tail_vec = tail_rows[edge_ids[2, 0:SPAN]]
    query_vec = rotate_query(head_vec, rel_rows)
    tail_image = rotate_tail(rel_rows, tail_vec)
    positive = jnp.sum(query_vec * tail_vec, axis=1)
    tail_side = side_terms(query_vec, positive, tail_rows[negative_ids[0, 1]])
    head_side = side_terms(tail_image, positive, head_rows[negative_ids[0, 0]])
    live_mask = (jnp.arange(SPAN, dtype=jnp.int32) + 0 < live_count).astype(jnp.float32)
    summed = jnp.sum(live_mask * (tail_side + head_side))
    return summed


def one_hot_rows(block_ids, choices_count):
    return (block_ids[..., None] == jnp.arange(choices_count, dtype=jnp.int32)).astype(jnp.float32)


def shards(
    head_table, tail_table, relations, edges, bucket_size, head_touched, tail_touched, negatives
):
    feature_columns = head_table.shape[2]
    head_count = lax.axis_size("head")
    tail_count = lax.axis_size("tail")
    tail_index = lax.axis_index("tail")
    head_slots = head_touched[0, 0]
    tail_slots = tail_touched[0, 0]

    local_blocks = head_table[0].reshape(-1, 128, feature_columns)
    blocks_here = local_blocks.shape[0]
    asked = lax.all_to_all(head_slots, "tail", 0, 0, tiled=True)
    sent_block = jnp.clip(asked - tail_index * blocks_here, 0, blocks_here - 1)
    outgoing = local_blocks[sent_block]
    head_rows = lax.all_to_all(outgoing, "tail", 0, 0, tiled=True)
    head_rows = jnp.where((head_slots >= 0)[:, None, None], head_rows, 0.0)

    tail_complete = lax.all_gather(tail_table[0], "head", axis=0, tiled=True)
    tail_selector = one_hot_rows(tail_slots, tail_complete.shape[0] // 128)
    tail_rows = jnp.einsum(
        "il,lov->iov",
        tail_selector,
        tail_complete.reshape(-1, 128, feature_columns),
        precision=TOP_PRECISION,
    )
    edge_ids = edges[0, 0]
    relation_ids = edge_ids[1]
    rel_rows = relations[relation_ids]

    def local_loss(head_flat, tail_flat, rel_flat):
        return edge_loss(
            head_flat, tail_flat, rel_flat, edge_ids, bucket_size[0, 0], negatives[0, 0]
        )

    loss_value, pullback = jax.vjp(
        local_loss,
        head_rows.reshape(-1, feature_columns),
        tail_rows.reshape(-1, feature_columns),
        rel_rows,
    )
    head_slot_gradient, tail_slot_gradient, rel_edge_grad = pullback(jnp.ones_like(loss_value))

    row_count = relations.shape[0]
    per_device = row_count // (head_count * tail_count)
    dense = jax.ops.segment_sum(rel_edge_grad, relation_ids, num_segments=row_count)
    stage = lax.psum_scatter(
        dense.reshape(head_count, tail_count * per_device, feature_columns),
        "head",
        scatter_dimension=0,
        tiled=True,
    ).reshape(tail_count, per_device, feature_columns)

    head_slot_gradient = jnp.where(
        (head_slots >= 0)[:, None, None],
        head_slot_gradient.reshape(-1, 128, feature_columns),
        0.0,
    )
    returned = lax.all_to_all(head_slot_gradient, "tail", 0, 0, tiled=True)
    returned_block = asked - tail_index * blocks_here
    head_result = jnp.stack(
        [
            jnp.sum(jnp.where((returned_block == j)[:, None, None], returned, 0.0), axis=0)
            for j in range(blocks_here)
        ]
    ).reshape(-1, feature_columns)

    tail_slot_gradient = tail_slot_gradient.reshape(-1, 128, feature_columns)
    tail_full_rows = jnp.einsum(
        "ip,iey->pey", tail_selector, tail_slot_gradient, precision=TOP_PRECISION
    ).reshape(-1, feature_columns)
    tail_result = lax.psum_scatter(tail_full_rows, "head", scatter_dimension=0, tiled=True)

    relation_result = jnp.sum(lax.all_to_all(stage, "tail", 0, 0, tiled=True), axis=0)
    return (
        head_result.reshape(1, -1, feature_columns),
        tail_result.reshape(1, -1, feature_columns),
        relation_result,
    )


def solution(mesh):
    in_specs = (
        P("head", "tail", None),
        P("tail", "head", None),
        P(),
        P("head", "tail", None, None),
        P("head", "tail"),
        P("head", "tail", None),
        P("head", "tail", None),
        P("head", "tail", None, None, None),
    )
    out_specs = (P("head", "tail", None), P("tail", "head", None), P(("head", "tail"), None))
    return jax.shard_map(shards, mesh=mesh, in_specs=in_specs, out_specs=out_specs, check_vma=False)
```

```python
import jax
import jax.numpy as jnp
from jax import lax
from jax.sharding import PartitionSpec as P

SPAN = 640


TOP_PRECISION = lax.Precision.HIGHEST


def rotate_query(head_vec, rel_vec):
    middle = head_vec.shape[1] // 2
    head_re, head_im = (head_vec[:, :middle], head_vec[:, middle:])
    rel_re, rel_im = (rel_vec[:, :middle], rel_vec[:, middle:])
    return jnp.concatenate(
        [head_re * rel_re + head_im * rel_im, head_im * rel_re - head_re * rel_im], axis=1
    )


def rotate_tail(rel_vec, tail_vec):
    middle = tail_vec.shape[1] // 2
    tail_re, tail_im = (tail_vec[:, :middle], tail_vec[:, middle:])
    rel_re, rel_im = (rel_vec[:, :middle], rel_vec[:, middle:])
    return jnp.concatenate(
        [rel_re * tail_re - rel_im * tail_im, rel_re * tail_im + rel_im * tail_re], axis=1
    )


def side_terms(query_vec, positive, candidates):
    scores = jnp.dot(query_vec, candidates.T, precision=TOP_PRECISION)
    weights = lax.stop_gradient(jax.nn.softmax(scores, axis=1))
    return jax.nn.softplus(-positive) + jnp.sum(weights * jax.nn.softplus(scores), axis=1)


def edge_loss(head_rows, tail_rows, rel_rows, edge_ids, live_count, negative_ids):
    head_vec = head_rows[edge_ids[0, 0:SPAN]]
    tail_vec = tail_rows[edge_ids[2, 0:SPAN]]
    query_vec = rotate_query(head_vec, rel_rows)
    tail_image = rotate_tail(rel_rows, tail_vec)
    positive = jnp.sum(query_vec * tail_vec, axis=1)
    tail_side = side_terms(query_vec, positive, tail_rows[negative_ids[0, 1]])
    head_side = side_terms(tail_image, positive, head_rows[negative_ids[0, 0]])
    live_mask = (jnp.arange(SPAN, dtype=jnp.int32) + 0 < live_count).astype(jnp.float32)
    summed = jnp.sum(live_mask * (tail_side + head_side))
    return summed


def one_hot_rows(block_ids, choices_count):
    return (block_ids[..., None] == jnp.arange(choices_count, dtype=jnp.int32)).astype(jnp.float32)


def shards(
    head_table, tail_table, relations, edges, bucket_size, head_touched, tail_touched, negatives
):
    feature_columns = head_table.shape[2]
    head_count = lax.axis_size("head")
    tail_count = lax.axis_size("tail")
    tail_index = lax.axis_index("tail")
    head_slots = head_touched[0, 0]
    tail_slots = tail_touched[0, 0]

    local_blocks = head_table[0].reshape(-1, 128, feature_columns)
    blocks_here = local_blocks.shape[0]
    asked = lax.all_to_all(head_slots, "tail", 0, 0, tiled=True)
    sent_block = jnp.clip(asked - tail_index * blocks_here, 0, blocks_here - 1)
    outgoing = local_blocks[sent_block]
    head_rows = lax.all_to_all(outgoing, "tail", 0, 0, tiled=True)
    head_rows = jnp.where((head_slots >= 0)[:, None, None], head_rows, 0.0)

    tail_complete = lax.all_gather(tail_table[0], "head", axis=0, tiled=True)
    tail_selector = one_hot_rows(tail_slots, tail_complete.shape[0] // 128)
    tail_blocks = tail_complete.reshape(-1, 128, feature_columns)
    tail_rows = jnp.take(tail_blocks, jnp.clip(tail_slots, 0, tail_blocks.shape[0] - 1), axis=0)
    tail_rows = jnp.where((tail_slots >= 0)[:, None, None], tail_rows, 0.0)
    edge_ids = edges[0, 0]
    relation_ids = edge_ids[1]
    rel_rows = relations[relation_ids]

    def local_loss(head_flat, tail_flat, rel_flat):
        return edge_loss(
            head_flat, tail_flat, rel_flat, edge_ids, bucket_size[0, 0], negatives[0, 0]
        )

    loss_value, pullback = jax.vjp(
        local_loss,
        head_rows.reshape(-1, feature_columns),
        tail_rows.reshape(-1, feature_columns),
        rel_rows,
    )
    head_slot_gradient, tail_slot_gradient, rel_edge_grad = pullback(jnp.ones_like(loss_value))

    row_count = relations.shape[0]
    per_device = row_count // (head_count * tail_count)
    dense = jax.ops.segment_sum(rel_edge_grad, relation_ids, num_segments=row_count)
    stage = lax.psum_scatter(
        dense.reshape(head_count, tail_count * per_device, feature_columns),
        "head",
        scatter_dimension=0,
        tiled=True,
    ).reshape(tail_count, per_device, feature_columns)

    head_slot_gradient = jnp.where(
        (head_slots >= 0)[:, None, None],
        head_slot_gradient.reshape(-1, 128, feature_columns),
        0.0,
    )
    both = jnp.concatenate([head_slot_gradient, stage], axis=1)
    both = lax.all_to_all(both, "tail", 0, 0, tiled=True)
    returned = both[:, :128]
    relation_result = jnp.sum(both[:, 128:], axis=0)
    returned_block = asked - tail_index * blocks_here
    head_result = jnp.stack(
        [
            jnp.sum(jnp.where((returned_block == j)[:, None, None], returned, 0.0), axis=0)
            for j in range(blocks_here)
        ]
    ).reshape(-1, feature_columns)

    tail_slot_gradient = tail_slot_gradient.reshape(-1, 128, feature_columns)
    tail_full_rows = jnp.einsum(
        "ip,iey->pey", tail_selector, tail_slot_gradient, precision=TOP_PRECISION
    ).reshape(-1, feature_columns)
    tail_result = lax.psum_scatter(tail_full_rows, "head", scatter_dimension=0, tiled=True)

    return (
        head_result.reshape(1, -1, feature_columns),
        tail_result.reshape(1, -1, feature_columns),
        relation_result,
    )


def solution(mesh):
    in_specs = (
        P("head", "tail", None),
        P("tail", "head", None),
        P(),
        P("head", "tail", None, None),
        P("head", "tail"),
        P("head", "tail", None),
        P("head", "tail", None),
        P("head", "tail", None, None, None),
    )
    out_specs = (P("head", "tail", None), P("tail", "head", None), P(("head", "tail"), None))
    return jax.shard_map(shards, mesh=mesh, in_specs=in_specs, out_specs=out_specs, check_vma=False)
```

```python
import jax
import jax.numpy as jnp
from jax import lax
from jax.sharding import PartitionSpec as P

SPAN = 640


TOP_PRECISION = lax.Precision.HIGHEST


def rotate_query(head_vec, rel_vec):
    middle = head_vec.shape[1] // 2
    head_re, head_im = (head_vec[:, :middle], head_vec[:, middle:])
    rel_re, rel_im = (rel_vec[:, :middle], rel_vec[:, middle:])
    return jnp.concatenate(
        [head_re * rel_re + head_im * rel_im, head_im * rel_re - head_re * rel_im], axis=1
    )


def rotate_tail(rel_vec, tail_vec):
    middle = tail_vec.shape[1] // 2
    tail_re, tail_im = (tail_vec[:, :middle], tail_vec[:, middle:])
    rel_re, rel_im = (rel_vec[:, :middle], rel_vec[:, middle:])
    return jnp.concatenate(
        [rel_re * tail_re - rel_im * tail_im, rel_re * tail_im + rel_im * tail_re], axis=1
    )


def side_terms(query_vec, positive, candidates):
    scores = jnp.dot(query_vec, candidates.T, precision=TOP_PRECISION)
    weights = lax.stop_gradient(jax.nn.softmax(scores, axis=1))
    return jax.nn.softplus(-positive) + jnp.sum(weights * jax.nn.softplus(scores), axis=1)


def edge_loss(head_rows, tail_rows, rel_rows, edge_ids, live_count, negative_ids):
    head_vec = head_rows[edge_ids[0, 0:SPAN]]
    tail_vec = tail_rows[edge_ids[2, 0:SPAN]]
    query_vec = rotate_query(head_vec, rel_rows)
    tail_image = rotate_tail(rel_rows, tail_vec)
    positive = jnp.sum(query_vec * tail_vec, axis=1)
    tail_side = side_terms(query_vec, positive, tail_rows[negative_ids[0, 1]])
    head_side = side_terms(tail_image, positive, head_rows[negative_ids[0, 0]])
    live_mask = (jnp.arange(SPAN, dtype=jnp.int32) + 0 < live_count).astype(jnp.float32)
    summed = jnp.sum(live_mask * (tail_side + head_side))
    return summed


def one_hot_rows(block_ids, choices_count):
    return (block_ids[..., None] == jnp.arange(choices_count, dtype=jnp.int32)).astype(jnp.float32)


def shards(
    head_table, tail_table, relations, edges, bucket_size, head_touched, tail_touched, negatives
):
    feature_columns = head_table.shape[2]
    head_count = lax.axis_size("head")
    tail_count = lax.axis_size("tail")
    tail_index = lax.axis_index("tail")
    head_slots = head_touched[0, 0]
    tail_slots = tail_touched[0, 0]

    local_blocks = head_table[0].reshape(-1, 128, feature_columns)
    blocks_here = local_blocks.shape[0]
    asked = lax.all_to_all(head_slots, "tail", 0, 0, tiled=True)
    sent_block = jnp.clip(asked - tail_index * blocks_here, 0, blocks_here - 1)
    outgoing = local_blocks[sent_block]
    head_rows = lax.all_to_all(outgoing, "tail", 0, 0, tiled=True)
    head_rows = jnp.where((head_slots >= 0)[:, None, None], head_rows, 0.0)

    tail_complete = lax.all_gather(tail_table[0], "head", axis=0, tiled=True)
    tail_selector = one_hot_rows(tail_slots, tail_complete.shape[0] // 128)
    tail_rows = jnp.einsum(
        "il,lov->iov",
        tail_selector,
        tail_complete.reshape(-1, 128, feature_columns),
        precision=TOP_PRECISION,
    )
    edge_ids = edges[0, 0]
    relation_ids = edge_ids[1]
    rel_rows = relations[relation_ids]

    def local_loss(head_flat, tail_flat, rel_flat):
        return edge_loss(
            head_flat, tail_flat, rel_flat, edge_ids, bucket_size[0, 0], negatives[0, 0]
        )

    loss_value, pullback = jax.vjp(
        local_loss,
        head_rows.reshape(-1, feature_columns),
        tail_rows.reshape(-1, feature_columns),
        rel_rows,
    )
    head_slot_gradient, tail_slot_gradient, rel_edge_grad = pullback(jnp.ones_like(loss_value))

    row_count = relations.shape[0]
    per_device = row_count // (head_count * tail_count)
    dense = jax.ops.segment_sum(rel_edge_grad, relation_ids, num_segments=row_count)
    stage = lax.psum_scatter(
        dense.reshape(head_count, tail_count * per_device, feature_columns),
        "head",
        scatter_dimension=0,
        tiled=True,
    ).reshape(tail_count, per_device, feature_columns)

    head_slot_gradient = jnp.where(
        (head_slots >= 0)[:, None, None],
        head_slot_gradient.reshape(-1, 128, feature_columns),
        0.0,
    )
    returned = lax.all_to_all(head_slot_gradient, "tail", 0, 0, tiled=True)
    returned_block = asked - tail_index * blocks_here
    head_result = jnp.stack(
        [
            jnp.sum(jnp.where((returned_block == j)[:, None, None], returned, 0.0), axis=0)
            for j in range(blocks_here)
        ]
    ).reshape(-1, feature_columns)

    tail_slot_gradient = tail_slot_gradient.reshape(-1, 128, feature_columns)
    tail_full_rows = jnp.einsum(
        "ip,iey->pey", tail_selector, tail_slot_gradient, precision=TOP_PRECISION
    ).reshape(-1, feature_columns)
    tail_result = lax.psum_scatter(tail_full_rows, "head", scatter_dimension=0, tiled=True)

    padded_rows = -(-per_device // 8) * 8
    stage = jnp.pad(stage, ((0, 0), (0, padded_rows - per_device), (0, 0)))
    relation_result = jnp.sum(lax.all_to_all(stage, "tail", 0, 0, tiled=True), axis=0)[:per_device]
    return (
        head_result.reshape(1, -1, feature_columns),
        tail_result.reshape(1, -1, feature_columns),
        relation_result,
    )


def solution(mesh):
    in_specs = (
        P("head", "tail", None),
        P("tail", "head", None),
        P(),
        P("head", "tail", None, None),
        P("head", "tail"),
        P("head", "tail", None),
        P("head", "tail", None),
        P("head", "tail", None, None, None),
    )
    out_specs = (P("head", "tail", None), P("tail", "head", None), P(("head", "tail"), None))
    return jax.shard_map(shards, mesh=mesh, in_specs=in_specs, out_specs=out_specs, check_vma=False)
```
